256 devices in a mesh: day: 8 (over x, core), row: 32 (over y, z).
Axes of the slice: x: 4, y: 4, z: 8, core: 2. Of those that a mesh axis runs over, the one named last changes fastest.
Arguments:
- features: bfloat16 [8, 768, 16, 128, 128], P('day', 'row'), may hold values from -6 to 6
- blocks: int32 [8, 768, 16], P('day', 'row'), may hold values from 0 to 255, as said below
- labels: int32 [8, 768, 128], P('day', 'row'), may hold values from 0 to 15
- coef: float32 [8, 16, 32768], P('day', None, 'row'), may hold values from -0.125 to 0.125
- direction: float32 [8, 16, 32768], P('day', None, 'row'), may hold values from -0.125 to 0.125
- prior: float32 [32768], P('row'), may hold values from 100 to 3000
Outputs:
- gradient: float32 [8, 16, 32768], P('day', None, 'row')
- hess_dir: float32 [8, 16, 32768], P('day', None, 'row')
The draws below stay inside these ranges and needn't reach their ends.
Inputs may be any that keep to these rules, and one draw needn't show every extreme that they name: `blocks`: within one row tile the 16 block numbers are distinct.
All inputs are finite; a program needn't handle non-finite values.
Results may differ from the reference program's by a relative error of at most 0.0003.
Values may be sent and summed in bfloat16 or wider, within the bound.
No kernel may reach another device: no remote copies, remote signals or barrier semaphores. Data moves between devices by JAX's collectives and lax.ppermute only.
A program may use at most 64 MiB of HBM per device.

```python
import math
import jax
import jax.numpy as jnp
from jax import lax

ARMS = 16
NBLK = 256
BW = 128
NACT = 16
TILE = 128
FEAT = 32768
TILES = 768
DAYS = 8


def draw_blocks(key, part):
    subkeys = jax.random.split(key, DAYS * TILES)
    chosen = jax.vmap(lambda subkey: jax.random.permutation(subkey, NBLK)[:NACT])(subkeys)
    return chosen.reshape(DAYS, TILES, NACT).astype(jnp.int32)


def set_ends(entries, key, smallest, high):
    longest = entries.shape.index(max(entries.shape))
    spots = []
    for shift in (0, 1):
        where = [jax.random.randint(jax.random.fold_in(key, axis), (), 0, length) for axis, length in enumerate(entries.shape)]
        where[longest] = (where[longest] + shift) % entries.shape[longest]
        spots.append(tuple(where))
    return entries.at[spots[0]].set(smallest).at[spots[1]].set(high)


def steps_of(rng, shape, cuts, smallest, largest):
    loudness = 1.0
    for axis_at, parts in cuts:
        draws = jax.random.uniform(jax.random.fold_in(jax.random.fold_in(rng, 6), axis_at), (parts,), jnp.float32, smallest / len(cuts), largest / len(cuts))
        loudness = loudness * jnp.repeat(jnp.exp(draws), shape[axis_at] // parts).reshape((-1,) + (1,) * (len(shape) - 1 - axis_at))
    return loudness


def centred(rng, extent, deviation, bound, pieces=(), held_as=jnp.bfloat16):
    values = jax.random.normal(rng, extent, jnp.float32) * deviation
    if len(pieces) > 0:
        values = steps_of(rng, extent, pieces, -0.22, 0.18) * values
    return jnp.clip(values, min=-bound, max=bound).astype(held_as)


def setup_inputs(seed: int = 0) -> dict:
    seeds = jax.random.split(jax.random.key(seed), 7)
    features = centred(seeds[0], (DAYS, TILES, NACT, TILE, BW), 1.0, 6.0, ((0, 8), (1, 32)))
    blocks = draw_blocks(jax.random.fold_in(seeds[6], 71), 0)
    labels = set_ends(jax.random.randint(seeds[2], (DAYS, TILES, TILE), 0, ARMS), jax.random.fold_in(seeds[2], 1), 0, ARMS - 1).astype(jnp.int32)
    coef = centred(seeds[3], (DAYS, ARMS, FEAT), (NACT * BW) ** -0.5, 0.125, ((0, 8), (2, 32)), jnp.float32)
    direction = centred(seeds[4], (DAYS, ARMS, FEAT), (NACT * BW) ** -0.5, 0.125, ((0, 8), (2, 32)), jnp.float32)
    prior = jnp.clip(jnp.exp(math.log(3000.0) - 3.4011974 * jax.random.uniform(seeds[5], (FEAT,), jnp.float32) ** steps_of(seeds[5], (FEAT,), ((0, 32),), -0.2, 0.2)), 100.0, 3000.0)
    return {"features": features, "blocks": blocks, "labels": labels, "coef": coef, "direction": direction, "prior": prior}


def day_terms(items):
    feats, blks, labs, coef_low, dir_low = items
    coef_pair = jnp.concatenate([coef_low, dir_low], axis=0)
    nfeat = coef_pair.shape[1]
    width = feats.shape[-1]
    coef_table = coef_pair.reshape(2 * ARMS, nfeat // width, width)
    selected = coef_table[:, blks]
    feats_wide = feats.astype(jnp.float32)
    logits_dir = jnp.einsum('tari,ktai->tkr', feats_wide, selected.astype(jnp.float32))
    logits = logits_dir[:, :ARMS]
    lin_dir = logits_dir[:, ARMS:]
    expo = jnp.exp(logits)
    probs = expo / jnp.sum(expo, axis=1, keepdims=True)
    onehot = (labs[:, None, :] == jnp.arange(ARMS, dtype=jnp.int32)[None, :, None]).astype(jnp.float32)
    resid = probs - onehot
    hrow = probs * lin_dir - probs * jnp.sum(probs * lin_dir, axis=1, keepdims=True)
    both_low = jnp.concatenate([resid, hrow], axis=1).astype(jnp.bfloat16)
    contrib = jnp.einsum('tari,tkr->ktai', feats_wide, both_low.astype(jnp.float32))
    summed = jnp.zeros((2 * ARMS, nfeat // width, width), jnp.float32)
    summed = summed.at[:, blks.reshape(-1)].add(contrib.reshape(2 * ARMS, -1, width))
    return summed.reshape(2 * ARMS, nfeat)


def reference(features, blocks, labels, coef, direction, prior):
    coef_low = coef.astype(jnp.bfloat16)
    dir_low = direction.astype(jnp.bfloat16)
    data_terms = lax.map(day_terms, (features, blocks, labels, coef_low, dir_low))
    both = jnp.concatenate([coef, direction], axis=1)
    zeros_day = jnp.zeros_like(both[:1])
    earlier = jnp.concatenate([zeros_day, both[:-1]], axis=0)
    later = jnp.concatenate([both[1:], zeros_day], axis=0)
    day_index = jnp.arange(DAYS, dtype=jnp.int32)
    links = ((day_index > 0).astype(jnp.float32) + (day_index < DAYS - 1).astype(jnp.float32))[:, None, None]
    result = data_terms + prior[None, None, :] * (links * both - earlier - later)
    return result[:, :ARMS], result[:, ARMS:]
```

```python
import jax
import jax.numpy as jnp
from jax import lax
from jax.sharding import Mesh
from jax.sharding import PartitionSpec as P

ROW = ("row_0", "row_1")


def extended(cells, sides, width):
    for axis, dim in sides:
        count = lax.axis_size(axis)
        ends = count - 1
        head = lax.slice_in_dim(cells, 0, width, axis=dim)
        tail = lax.slice_in_dim(cells, cells.shape[dim] - width, cells.shape[dim], axis=dim)
        cells = jnp.concatenate(
            [
                lax.ppermute(tail, axis, [(i, (i + 1) % count) for i in range(ends)]),
                cells,
                lax.ppermute(head, axis, [((i + 1) % count, i) for i in range(ends)]),
            ],
            axis=dim,
        )
    return cells


def on_device(features, blocks, labels, coef, direction, prior):
    arms = coef.shape[1]
    width = features.shape[-1]
    coef_pair = jnp.concatenate([coef[0], direction[0]], axis=0).astype(jnp.bfloat16)
    coef_table = lax.all_gather(coef_pair, ROW, axis=1, tiled=True)
    nfeat = coef_table.shape[1]
    nblk = nfeat // width
    both = jnp.concatenate([coef, direction], axis=1)
    neighbours = extended(both, (("day", 0),), 1)
    blks = blocks[0]
    selected = coef_table.reshape(2 * arms, nblk, width)[:, blks]
    feats = features[0]
    logits_dir = jnp.einsum("tari,ktai->tkr", feats, selected, preferred_element_type=jnp.float32)
    logits = logits_dir[:, :arms]
    lin_dir = logits_dir[:, arms:]
    expo = jnp.exp(logits)
    probs = expo / jnp.sum(expo, axis=1, keepdims=True)
    onehot = (labels[0][:, None, :] == jnp.arange(arms, dtype=jnp.int32)[None, :, None]).astype(
        jnp.float32
    )
    resid = probs - onehot
    hrow = probs * lin_dir - probs * jnp.sum(probs * lin_dir, axis=1, keepdims=True)
    both_low = jnp.concatenate([resid, hrow], axis=1).astype(jnp.bfloat16)
    contrib = jnp.einsum("tari,tkr->taki", feats, both_low, preferred_element_type=jnp.float32)
    contrib = contrib.reshape(-1, 2 * arms, width)
    top = lax.reduce_precision(contrib, exponent_bits=8, mantissa_bits=7)
    hi = top.astype(jnp.bfloat16)
    lo = (contrib - top).astype(jnp.bfloat16)
    place = (blks.reshape(-1)[:, None] == jnp.arange(nblk, dtype=jnp.int32)[None, :]).astype(
        jnp.bfloat16
    )
    parts = jnp.einsum(
        "pb,pjki->jkbi", place, jnp.stack([hi, lo], axis=1), preferred_element_type=jnp.float32
    )
    partial_terms = parts[0] + parts[1]
    partial_terms = partial_terms.reshape(2 * arms, nfeat)
    owned = lax.psum_scatter(partial_terms, ROW, scatter_dimension=1, tiled=True)
    day_index = lax.axis_index("day")
    ndays = lax.axis_size("day")
    links = (day_index > 0).astype(jnp.float32) + (day_index < ndays - 1).astype(jnp.float32)
    coupling = links * neighbours[1] - neighbours[0] - neighbours[2]
    result = owned + prior[None, :] * coupling
    return (result[None, :arms], result[None, arms:])


def solution(mesh):
    finer = Mesh(mesh.devices.reshape(mesh.shape["day"], 4, 8), ("day", "row_0", "row_1"))
    return jax.shard_map(
        on_device,
        mesh=finer,
        in_specs=(
            P("day", ROW, None, None, None),
            P("day", ROW, None),
            P("day", ROW, None),
            P("day", None, ROW),
            P("day", None, ROW),
            P(ROW),
        ),
        out_specs=(P("day", None, ROW), P("day", None, ROW)),
        check_vma=False,
    )
```

```python
import jax
import jax.numpy as jnp
from jax import lax
from jax.sharding import Mesh
from jax.sharding import PartitionSpec as P

ROW = ("row_0", "row_1")


def copy_for_each(value, axis):
    copies = jnp.broadcast_to(value, (lax.axis_size(axis), *value.shape))
    return lax.all_to_all(copies, axis, split_axis=0, concat_axis=0, tiled=True)


def extended(cells, sides, width):
    for axis, dim in sides:
        count = lax.axis_size(axis)
        ends = count - 1
        head = lax.slice_in_dim(cells, 0, width, axis=dim)
        tail = lax.slice_in_dim(cells, cells.shape[dim] - width, cells.shape[dim], axis=dim)
        cells = jnp.concatenate(
            [
                lax.ppermute(tail, axis, [(i, (i + 1) % count) for i in range(ends)]),
                cells,
                lax.ppermute(head, axis, [((i + 1) % count, i) for i in range(ends)]),
            ],
            axis=dim,
        )
    return cells


def scatter_axes(value, axes, dim):
    if not axes:
        return value
    nearer = lax.psum_scatter(value, axes[0], scatter_dimension=dim, tiled=True)
    return scatter_axes(nearer, axes[1:], dim)


def on_device(features, blocks, labels, coef, direction, prior):
    arms = coef.shape[1]
    width = features.shape[-1]
    coef_pair = jnp.concatenate([coef[0], direction[0]], axis=0).astype(jnp.bfloat16)
    local_blk = coef_pair.shape[1] // width
    by_block = coef_pair.reshape(2 * arms, local_blk, width).transpose(1, 0, 2)
    parts = copy_for_each(by_block, ROW)
    coef_table = parts.reshape(-1, 2 * arms, width)
    nblk = coef_table.shape[0]
    both = jnp.concatenate([coef, direction], axis=1)
    neighbours = extended(both, (("day", 0),), 1)
    blks = blocks[0]
    selected = coef_table[blks]
    feats = features[0]
    logits_dir = jnp.einsum("tari,taki->tkr", feats, selected, preferred_element_type=jnp.float32)
    logits = logits_dir[:, :arms]
    lin_dir = logits_dir[:, arms:]
    expo = jnp.exp(logits)
    probs = expo / jnp.sum(expo, axis=1, keepdims=True)
    onehot = (labels[0][:, None, :] == jnp.arange(arms, dtype=jnp.int32)[None, :, None]).astype(
        jnp.float32
    )
    resid = probs - onehot
    hrow = probs * lin_dir - probs * jnp.sum(probs * lin_dir, axis=1, keepdims=True)
    both_low = jnp.concatenate([resid, hrow], axis=1).astype(jnp.bfloat16)
    contrib = jnp.einsum("tari,tkr->taki", feats, both_low, preferred_element_type=jnp.float32)
    contrib = contrib.reshape(-1, 2 * arms * width)
    top = lax.reduce_precision(contrib, exponent_bits=8, mantissa_bits=7)
    hi = top.astype(jnp.bfloat16)
    lo = (contrib - top).astype(jnp.bfloat16)
    place = (jnp.arange(nblk, dtype=jnp.int32)[:, None] == blks.reshape(-1)[None, :]).astype(
        jnp.bfloat16
    )
    split = jnp.einsum(
        "bp,jpc->jbc", place, jnp.stack([hi, lo], axis=0), preferred_element_type=jnp.float32
    )
    partial_terms = (split[0] + split[1]).reshape(nblk, 2 * arms, width)
    owned = scatter_axes(partial_terms, ROW, 0)
    owned = owned.transpose(1, 0, 2).reshape(2 * arms, -1)
    day_index = lax.axis_index("day")
    ndays = lax.axis_size("day")
    links = (day_index > 0).astype(jnp.float32) + (day_index < ndays - 1).astype(jnp.float32)
    coupling = links * neighbours[1] - neighbours[0] - neighbours[2]
    result = owned + prior[None, :] * coupling
    return (result[None, :arms], result[None, arms:])


def solution(mesh):
    finer = Mesh(mesh.devices.reshape(mesh.shape["day"], 4, 8), ("day", "row_0", "row_1"))
    return jax.shard_map(
        on_device,
        mesh=finer,
        in_specs=(
            P("day", ROW, None, None, None),
            P("day", ROW, None),
            P("day", ROW, None),
            P("day", None, ROW),
            P("day", None, ROW),
            P(ROW),
        ),
        out_specs=(P("day", None, ROW), P("day", None, ROW)),
        check_vma=False,
    )
```

```python
import jax
import jax.numpy as jnp
from jax import lax
from jax.sharding import Mesh
from jax.sharding import PartitionSpec as P

ROW = ("row_0", "row_1")


def copy_for_each(value, axis):
    copies = jnp.broadcast_to(value, (lax.axis_size(axis), *value.shape))
    return lax.all_to_all(copies, axis, split_axis=0, concat_axis=0, tiled=True)


def extended(cells, sides, width):
    for axis, dim in sides:
        count = lax.axis_size(axis)
        ends = count - 1
        head = lax.slice_in_dim(cells, 0, width, axis=dim)
        tail = lax.slice_in_dim(cells, cells.shape[dim] - width, cells.shape[dim], axis=dim)
        cells = jnp.concatenate(
            [
                lax.ppermute(tail, axis, [(i, (i + 1) % count) for i in range(ends)]),
                cells,
                lax.ppermute(head, axis, [((i + 1) % count, i) for i in range(ends)]),
            ],
            axis=dim,
        )
    return cells


def scatter_axes(value, axes, dim):
    if not axes:
        return value
    nearer = lax.psum_scatter(value, axes[0], scatter_dimension=dim, tiled=True)
    return scatter_axes(nearer, axes[1:], dim)


def on_device(features, blocks, labels, coef, direction, prior):
    arms = coef.shape[1]
    width = features.shape[-1]
    coef_pair = jnp.concatenate([coef[0], direction[0]], axis=0).astype(jnp.bfloat16)
    local_blk = coef_pair.shape[1] // width
    by_block = coef_pair.reshape(2 * arms, local_blk, width).transpose(1, 0, 2)
    coef_table = lax.all_gather(by_block, "row_1", axis=0, tiled=True)
    coef_table = lax.all_gather(coef_table, "row_0", axis=0, tiled=True)
    nblk = coef_table.shape[0]
    both = jnp.concatenate([coef, direction], axis=1)
    neighbours = extended(both, (("day", 0),), 1)
    blks = blocks[0]
    selected = coef_table[blks]
    feats = features[0]
    logits_dir = jnp.einsum("tari,taki->tkr", feats, selected, preferred_element_type=jnp.float32)
    logits = logits_dir[:, :arms]
    lin_dir = logits_dir[:, arms:]
    expo = jnp.exp(logits)
    probs = expo / jnp.sum(expo, axis=1, keepdims=True)
    onehot = (labels[0][:, None, :] == jnp.arange(arms, dtype=jnp.int32)[None, :, None]).astype(
        jnp.float32
    )
    resid = probs - onehot
    hrow = probs * lin_dir - probs * jnp.sum(probs * lin_dir, axis=1, keepdims=True)
    both_low = jnp.concatenate([resid, hrow], axis=1).astype(jnp.bfloat16)
    contrib = jnp.einsum("tari,tkr->taki", feats, both_low, preferred_element_type=jnp.float32)
    contrib = contrib.reshape(-1, 2 * arms * width)
    top = lax.reduce_precision(contrib, exponent_bits=8, mantissa_bits=7)
    hi = top.astype(jnp.bfloat16)
    lo = (contrib - top).astype(jnp.bfloat16)
    outer = lax.axis_size("row_0")
    inner = lax.axis_size("row_1")
    order = jnp.arange(nblk, dtype=jnp.int32).reshape(outer, inner, -1).transpose(1, 0, 2)
    place = (order.reshape(-1)[:, None] == blks.reshape(-1)[None, :]).astype(jnp.bfloat16)
    split = jnp.einsum(
        "bp,jpc->jbc", place, jnp.stack([hi, lo], axis=0), preferred_element_type=jnp.float32
    )
    partial_terms = (split[0] + split[1]).reshape(nblk, 2 * arms, width)
    owned = lax.psum_scatter(partial_terms, "row_1", scatter_dimension=0, tiled=True)
    owned = lax.psum_scatter(owned, "row_0", scatter_dimension=0, tiled=True)
    owned = owned.transpose(1, 0, 2).reshape(2 * arms, -1)
    day_index = lax.axis_index("day")
    ndays = lax.axis_size("day")
    links = (day_index > 0).astype(jnp.float32) + (day_index < ndays - 1).astype(jnp.float32)
    coupling = links * neighbours[1] - neighbours[0] - neighbours[2]
    result = owned + prior[None, :] * coupling
    return (result[None, :arms], result[None, arms:])


def solution(mesh):
    finer = Mesh(mesh.devices.reshape(mesh.shape["day"], 4, 8), ("day", "row_0", "row_1"))
    return jax.shard_map(
        on_device,
        mesh=finer,
        in_specs=(
            P("day", ROW, None, None, None),
            P("day", ROW, None),
            P("day", ROW, None),
            P("day", None, ROW),
            P("day", None, ROW),
            P(ROW),
        ),
        out_specs=(P("day", None, ROW), P("day", None, ROW)),
        check_vma=False,
    )
```

```python
import jax
import jax.numpy as jnp
from jax import lax
from jax.sharding import Mesh
from jax.sharding import PartitionSpec as P
from jax.experimental import pallas as pl
from jax.experimental.pallas import tpu as pltpu

ROW = ("row_0", "row_1")


def copy_for_each(value, axis):
    copies = jnp.broadcast_to(value, (lax.axis_size(axis), *value.shape))
    return lax.all_to_all(copies, axis, split_axis=0, concat_axis=0, tiled=True)


def extended(cells, sides, width):
    for axis, dim in sides:
        count = lax.axis_size(axis)
        ends = count - 1
        head = lax.slice_in_dim(cells, 0, width, axis=dim)
        tail = lax.slice_in_dim(cells, cells.shape[dim] - width, cells.shape[dim], axis=dim)
        cells = jnp.concatenate(
            [
                lax.ppermute(tail, axis, [(i, (i + 1) % count) for i in range(ends)]),
                cells,
                lax.ppermute(head, axis, [((i + 1) % count, i) for i in range(ends)]),
            ],
            axis=dim,
        )
    return cells


def scatter_axes(value, axes, dim):
    if not axes:
        return value
    nearer = lax.psum_scatter(value, axes[0], scatter_dimension=dim, tiled=True)
    return scatter_axes(nearer, axes[1:], dim)


def scatter_kernel(dest_ref, part_ref, out_ref):
    t = pl.program_id(0)
    slots = part_ref.shape[1]

    @pl.when(t == 0)
    def _():
        out_ref[...] = jnp.zeros_like(out_ref)

    for a in range(slots):
        q = dest_ref[t * slots + a]
        out_ref[q] = out_ref[q] + part_ref[0, a]


def scatter_rows(dest, contrib, nblk):
    tiles, slots, rows, width = contrib.shape
    return pl.pallas_call(
        scatter_kernel,
        grid_spec=pltpu.PrefetchScalarGridSpec(
            num_scalar_prefetch=1,
            grid=(tiles,),
            in_specs=[pl.BlockSpec((1, slots, rows, width), lambda t, d: (t, 0, 0, 0))],
            out_specs=pl.BlockSpec((nblk, rows, width), lambda t, d: (0, 0, 0)),
        ),
        out_shape=jax.ShapeDtypeStruct((nblk, rows, width), jnp.float32),
        compiler_params=pltpu.CompilerParams(
            dimension_semantics=("arbitrary",), vmem_limit_bytes=40 * 1024 * 1024
        ),
    )(dest, contrib)


def on_device(features, blocks, labels, coef, direction, prior):
    arms = coef.shape[1]
    width = features.shape[-1]
    coef_pair = jnp.concatenate([coef[0], direction[0]], axis=0).astype(jnp.bfloat16)
    local_blk = coef_pair.shape[1] // width
    by_block = coef_pair.reshape(2 * arms, local_blk, width).transpose(1, 0, 2)
    coef_table = lax.all_gather(by_block, "row_1", axis=0, tiled=True)
    coef_table = lax.all_gather(coef_table, "row_0", axis=0, tiled=True)
    nblk = coef_table.shape[0]
    both = jnp.concatenate([coef, direction], axis=1)
    neighbours = extended(both, (("day", 0),), 1)
    blks = blocks[0]
    selected = coef_table[blks]
    feats = features[0]
    logits_dir = jnp.einsum("tari,taki->tkr", feats, selected, preferred_element_type=jnp.float32)
    logits = logits_dir[:, :arms]
    lin_dir = logits_dir[:, arms:]
    expo = jnp.exp(logits)
    probs = expo / jnp.sum(expo, axis=1, keepdims=True)
    onehot = (labels[0][:, None, :] == jnp.arange(arms, dtype=jnp.int32)[None, :, None]).astype(
        jnp.float32
    )
    resid = probs - onehot
    hrow = probs * lin_dir - probs * jnp.sum(probs * lin_dir, axis=1, keepdims=True)
    both_low = jnp.concatenate([resid, hrow], axis=1).astype(jnp.bfloat16)
    contrib = jnp.einsum("tari,tkr->taki", feats, both_low, preferred_element_type=jnp.float32)
    outer = lax.axis_size("row_0")
    inner = lax.axis_size("row_1")
    per = nblk // (outer * inner)
    flat = blks.reshape(-1)
    dest = ((flat // per) % inner) * (outer * per) + (flat // (inner * per)) * per + flat % per
    partial_terms = scatter_rows(dest, contrib, nblk)
    owned = lax.psum_scatter(partial_terms, "row_1", scatter_dimension=0, tiled=True)
    owned = lax.psum_scatter(owned, "row_0", scatter_dimension=0, tiled=True)
    owned = owned.transpose(1, 0, 2).reshape(2 * arms, -1)
    day_index = lax.axis_index("day")
    ndays = lax.axis_size("day")
    links = (day_index > 0).astype(jnp.float32) + (day_index < ndays - 1).astype(jnp.float32)
    coupling = links * neighbours[1] - neighbours[0] - neighbours[2]
    result = owned + prior[None, :] * coupling
    return (result[None, :arms], result[None, arms:])


def solution(mesh):
    finer = Mesh(mesh.devices.reshape(mesh.shape["day"], 4, 8), ("day", "row_0", "row_1"))
    return jax.shard_map(
        on_device,
        mesh=finer,
        in_specs=(
            P("day", ROW, None, None, None),
            P("day", ROW, None),
            P("day", ROW, None),
            P("day", None, ROW),
            P("day", None, ROW),
            P(ROW),
        ),
        out_specs=(P("day", None, ROW), P("day", None, ROW)),
        check_vma=False,
    )
```

```python
import jax
import jax.numpy as jnp
from jax import lax
from jax.sharding import Mesh
from jax.sharding import PartitionSpec as P
from jax.experimental import pallas as pl
from jax.experimental.pallas import tpu as pltpu

ROW = ("row_0", "row_1")


def copy_for_each(value, axis):
    copies = jnp.broadcast_to(value, (lax.axis_size(axis), *value.shape))
    return lax.all_to_all(copies, axis, split_axis=0, concat_axis=0, tiled=True)


def extended(cells, sides, width):
    for axis, dim in sides:
        count = lax.axis_size(axis)
        ends = count - 1
        head = lax.slice_in_dim(cells, 0, width, axis=dim)
        tail = lax.slice_in_dim(cells, cells.shape[dim] - width, cells.shape[dim], axis=dim)
        cells = jnp.concatenate(
            [
                lax.ppermute(tail, axis, [(i, (i + 1) % count) for i in range(ends)]),
                cells,
                lax.ppermute(head, axis, [((i + 1) % count, i) for i in range(ends)]),
            ],
            axis=dim,
        )
    return cells


def scatter_axes(value, axes, dim):
    if not axes:
        return value
    nearer = lax.psum_scatter(value, axes[0], scatter_dimension=dim, tiled=True)
    return scatter_axes(nearer, axes[1:], dim)


def scatter_kernel(dest_ref, part_ref, out_ref):
    t = pl.program_id(0)
    slots = part_ref.shape[1]

    @pl.when(t == 0)
    def _():
        out_ref[...] = jnp.zeros_like(out_ref)

    for a in range(slots):
        q = dest_ref[t * slots + a]
        out_ref[q] = out_ref[q] + part_ref[0, a]


def scatter_rows(dest, contrib, nblk):
    tiles, slots, rows, width = contrib.shape
    return pl.pallas_call(
        scatter_kernel,
        grid_spec=pltpu.PrefetchScalarGridSpec(
            num_scalar_prefetch=1,
            grid=(tiles,),
            in_specs=[pl.BlockSpec((1, slots, rows, width), lambda t, d: (t, 0, 0, 0))],
            out_specs=pl.BlockSpec((nblk, rows, width), lambda t, d: (0, 0, 0)),
        ),
        out_shape=jax.ShapeDtypeStruct((nblk, rows, width), jnp.float32),
        compiler_params=pltpu.CompilerParams(
            dimension_semantics=("arbitrary",), vmem_limit_bytes=40 * 1024 * 1024
        ),
    )(dest, contrib)


def on_device(features, blocks, labels, coef, direction, prior):
    arms = coef.shape[1]
    width = features.shape[-1]
    coef_pair = jnp.concatenate([coef[0], direction[0]], axis=0).astype(jnp.bfloat16)
    local_blk = coef_pair.shape[1] // width
    by_block = coef_pair.reshape(2 * arms, local_blk, width).transpose(1, 0, 2)
    here = lax.axis_index("row_1")
    count = lax.axis_size("row_1")
    pieces = [by_block] + [
        lax.ppermute(by_block, "row_1", [(i, (i + s) % count) for i in range(count)])
        for s in range(1, count)
    ]
    coef_table = lax.all_gather(jnp.concatenate(pieces, axis=0), "row_0", axis=0, tiled=True)
    nblk = coef_table.shape[0]
    both = jnp.concatenate([coef, direction], axis=1)
    neighbours = extended(both, (("day", 0),), 1)
    blks = blocks[0]
    span = count * local_blk
    rotated = (blks // span) * span + ((here - (blks // local_blk) % count) % count) * local_blk
    selected = coef_table[rotated + blks % local_blk]
    feats = features[0]
    logits_dir = jnp.einsum("tari,taki->tkr", feats, selected, preferred_element_type=jnp.float32)
    logits = logits_dir[:, :arms]
    lin_dir = logits_dir[:, arms:]
    expo = jnp.exp(logits)
    probs = expo / jnp.sum(expo, axis=1, keepdims=True)
    onehot = (labels[0][:, None, :] == jnp.arange(arms, dtype=jnp.int32)[None, :, None]).astype(
        jnp.float32
    )
    resid = probs - onehot
    hrow = probs * lin_dir - probs * jnp.sum(probs * lin_dir, axis=1, keepdims=True)
    both_low = jnp.concatenate([resid, hrow], axis=1).astype(jnp.bfloat16)
    contrib = jnp.einsum("tari,tkr->taki", feats, both_low, preferred_element_type=jnp.float32)
    outer = lax.axis_size("row_0")
    inner = lax.axis_size("row_1")
    per = nblk // (outer * inner)
    flat = blks.reshape(-1)
    dest = ((flat // per) % inner) * (outer * per) + (flat // (inner * per)) * per + flat % per
    partial_terms = scatter_rows(dest, contrib, nblk)
    owned = lax.psum_scatter(partial_terms, "row_1", scatter_dimension=0, tiled=True)
    owned = lax.psum_scatter(owned, "row_0", scatter_dimension=0, tiled=True)
    owned = owned.transpose(1, 0, 2).reshape(2 * arms, -1)
    day_index = lax.axis_index("day")
    ndays = lax.axis_size("day")
    links = (day_index > 0).astype(jnp.float32) + (day_index < ndays - 1).astype(jnp.float32)
    coupling = links * neighbours[1] - neighbours[0] - neighbours[2]
    result = owned + prior[None, :] * coupling
    return (result[None, :arms], result[None, arms:])


def solution(mesh):
    finer = Mesh(mesh.devices.reshape(mesh.shape["day"], 4, 8), ("day", "row_0", "row_1"))
    return jax.shard_map(
        on_device,
        mesh=finer,
        in_specs=(
            P("day", ROW, None, None, None),
            P("day", ROW, None),
            P("day", ROW, None),
            P("day", None, ROW),
            P("day", None, ROW),
            P(ROW),
        ),
        out_specs=(P("day", None, ROW), P("day", None, ROW)),
        check_vma=False,
    )
```

```python
import jax
import jax.numpy as jnp
from jax import lax
from jax.sharding import Mesh
from jax.sharding import PartitionSpec as P
from jax.experimental import pallas as pl
from jax.experimental.pallas import tpu as pltpu

ROW = ("row_0", "row_1")


def copy_for_each(value, axis):
    copies = jnp.broadcast_to(value, (lax.axis_size(axis), *value.shape))
    return lax.all_to_all(copies, axis, split_axis=0, concat_axis=0, tiled=True)


def extended(cells, sides, width):
    for axis, dim in sides:
        count = lax.axis_size(axis)
        ends = count - 1
        head = lax.slice_in_dim(cells, 0, width, axis=dim)
        tail = lax.slice_in_dim(cells, cells.shape[dim] - width, cells.shape[dim], axis=dim)
        cells = jnp.concatenate(
            [
                lax.ppermute(tail, axis, [(i, (i + 1) % count) for i in range(ends)]),
                cells,
                lax.ppermute(head, axis, [((i + 1) % count, i) for i in range(ends)]),
            ],
            axis=dim,
        )
    return cells


def scatter_axes(value, axes, dim):
    if not axes:
        return value
    nearer = lax.psum_scatter(value, axes[0], scatter_dimension=dim, tiled=True)
    return scatter_axes(nearer, axes[1:], dim)


def scatter_kernel(dest_ref, part_ref, out_ref):
    t = pl.program_id(0)
    slots = part_ref.shape[1]

    @pl.when(t == 0)
    def _():
        out_ref[...] = jnp.zeros_like(out_ref)

    for a in range(slots):
        q = dest_ref[t * slots + a]
        out_ref[q] = out_ref[q] + part_ref[0, a]


def scatter_rows(dest, contrib, nblk):
    tiles, slots, rows, width = contrib.shape
    return pl.pallas_call(
        scatter_kernel,
        grid_spec=pltpu.PrefetchScalarGridSpec(
            num_scalar_prefetch=1,
            grid=(tiles,),
            in_specs=[pl.BlockSpec((1, slots, rows, width), lambda t, d: (t, 0, 0, 0))],
            out_specs=pl.BlockSpec((nblk, rows, width), lambda t, d: (0, 0, 0)),
        ),
        out_shape=jax.ShapeDtypeStruct((nblk, rows, width), jnp.float32),
        compiler_params=pltpu.CompilerParams(
            dimension_semantics=("arbitrary",), vmem_limit_bytes=40 * 1024 * 1024
        ),
    )(dest, contrib)


def on_device(features, blocks, labels, coef, direction, prior):
    arms = coef.shape[1]
    width = features.shape[-1]
    coef_pair = jnp.concatenate([coef[0], direction[0]], axis=0).astype(jnp.bfloat16)
    local_blk = coef_pair.shape[1] // width
    by_block = coef_pair.reshape(2 * arms, local_blk, width).transpose(1, 0, 2)
    here = lax.axis_index("row_1")
    count = lax.axis_size("row_1")
    pieces = [by_block] + [
        lax.ppermute(by_block, "row_1", [(i, (i + s) % count) for i in range(count)])
        for s in range(1, count)
    ]
    stage = jnp.concatenate(pieces, axis=0)
    there = lax.axis_index("row_0")
    around = lax.axis_size("row_0")
    coef_table = jnp.concatenate(
        [stage]
        + [
            lax.ppermute(stage, "row_0", [(i, (i + s) % around) for i in range(around)])
            for s in range(1, around)
        ],
        axis=0,
    )
    nblk = coef_table.shape[0]
    both = jnp.concatenate([coef, direction], axis=1)
    neighbours = extended(both, (("day", 0),), 1)
    blks = blocks[0]
    span = count * local_blk
    rotated = ((there - blks // span) % around) * span + (
        (here - (blks // local_blk) % count) % count
    ) * local_blk
    selected = coef_table[rotated + blks % local_blk]
    feats = features[0]
    logits_dir = jnp.einsum("tari,taki->tkr", feats, selected, preferred_element_type=jnp.float32)
    logits = logits_dir[:, :arms]
    lin_dir = logits_dir[:, arms:]
    expo = jnp.exp(logits)
    probs = expo / jnp.sum(expo, axis=1, keepdims=True)
    onehot = (labels[0][:, None, :] == jnp.arange(arms, dtype=jnp.int32)[None, :, None]).astype(
        jnp.float32
    )
    resid = probs - onehot
    hrow = probs * lin_dir - probs * jnp.sum(probs * lin_dir, axis=1, keepdims=True)
    both_low = jnp.concatenate([resid, hrow], axis=1).astype(jnp.bfloat16)
    contrib = jnp.einsum("tari,tkr->taki", feats, both_low, preferred_element_type=jnp.float32)
    outer = lax.axis_size("row_0")
    inner = lax.axis_size("row_1")
    per = nblk // (outer * inner)
    flat = blks.reshape(-1)
    dest = ((flat // per) % inner) * (outer * per) + (flat // (inner * per)) * per + flat % per
    partial_terms = scatter_rows(dest, contrib, nblk)
    owned = lax.psum_scatter(partial_terms, "row_1", scatter_dimension=0, tiled=True)
    chunks = owned.reshape(around, -1, 2 * arms, width)
    total = chunks[there]
    for s in range(1, around):
        total = total + lax.ppermute(
            chunks[(there + s) % around], "row_0", [(i, (i + s) % around) for i in range(around)]
        )
    owned = total
    owned = owned.transpose(1, 0, 2).reshape(2 * arms, -1)
    day_index = lax.axis_index("day")
    ndays = lax.axis_size("day")
    links = (day_index > 0).astype(jnp.float32) + (day_index < ndays - 1).astype(jnp.float32)
    coupling = links * neighbours[1] - neighbours[0] - neighbours[2]
    result = owned + prior[None, :] * coupling
    return (result[None, :arms], result[None, arms:])


def solution(mesh):
    finer = Mesh(mesh.devices.reshape(mesh.shape["day"], 4, 8), ("day", "row_0", "row_1"))
    return jax.shard_map(
        on_device,
        mesh=finer,
        in_specs=(
            P("day", ROW, None, None, None),
            P("day", ROW, None),
            P("day", ROW, None),
            P("day", None, ROW),
            P("day", None, ROW),
            P(ROW),
        ),
        out_specs=(P("day", None, ROW), P("day", None, ROW)),
        check_vma=False,
    )
```

```python
import jax
import jax.numpy as jnp
from jax import lax
from jax.sharding import Mesh
from jax.sharding import PartitionSpec as P
from jax.experimental import pallas as pl
from jax.experimental.pallas import tpu as pltpu

ROW = ("row_0", "row_1")


def copy_for_each(value, axis):
    copies = jnp.broadcast_to(value, (lax.axis_size(axis), *value.shape))
    return lax.all_to_all(copies, axis, split_axis=0, concat_axis=0, tiled=True)


def extended(cells, sides, width):
    for axis, dim in sides:
        count = lax.axis_size(axis)
        ends = count - 1
        head = lax.slice_in_dim(cells, 0, width, axis=dim)
        tail = lax.slice_in_dim(cells, cells.shape[dim] - width, cells.shape[dim], axis=dim)
        cells = jnp.concatenate(
            [
                lax.ppermute(tail, axis, [(i, (i + 1) % count) for i in range(ends)]),
                cells,
                lax.ppermute(head, axis, [((i + 1) % count, i) for i in range(ends)]),
            ],
            axis=dim,
        )
    return cells


def scatter_axes(value, axes, dim):
    if not axes:
        return value
    nearer = lax.psum_scatter(value, axes[0], scatter_dimension=dim, tiled=True)
    return scatter_axes(nearer, axes[1:], dim)


def scatter_kernel(dest_ref, part_ref, out_ref):
    t = pl.program_id(0)
    slots = part_ref.shape[1]

    @pl.when(t == 0)
    def _():
        out_ref[...] = jnp.zeros_like(out_ref)

    for a in range(slots):
        q = dest_ref[t * slots + a]
        out_ref[q] = out_ref[q] + part_ref[0, a]


def scatter_rows(dest, contrib, nblk):
    tiles, slots, rows, width = contrib.shape
    return pl.pallas_call(
        scatter_kernel,
        grid_spec=pltpu.PrefetchScalarGridSpec(
            num_scalar_prefetch=1,
            grid=(tiles,),
            in_specs=[pl.BlockSpec((1, slots, rows, width), lambda t, d: (t, 0, 0, 0))],
            out_specs=pl.BlockSpec((nblk, rows, width), lambda t, d: (0, 0, 0)),
        ),
        out_shape=jax.ShapeDtypeStruct((nblk, rows, width), jnp.float32),
        compiler_params=pltpu.CompilerParams(
            dimension_semantics=("arbitrary",), vmem_limit_bytes=40 * 1024 * 1024
        ),
    )(dest, contrib)


def on_device(features, blocks, labels, coef, direction, prior):
    arms = coef.shape[1]
    width = features.shape[-1]
    coef_pair = jnp.concatenate([coef[0], direction[0]], axis=0).astype(jnp.bfloat16)
    local_blk = coef_pair.shape[1] // width
    by_block = coef_pair.reshape(2 * arms, local_blk, width).transpose(1, 0, 2)
    here = lax.axis_index("row_1")
    count = lax.axis_size("row_1")
    pieces = [by_block] + [
        lax.ppermute(by_block, "row_1", [(i, (i + s) % count) for i in range(count)])
        for s in range(1, count)
    ]
    stage = jnp.concatenate(pieces, axis=0)
    there = lax.axis_index("row_0")
    around = lax.axis_size("row_0")
    coef_table = jnp.concatenate(
        [stage]
        + [
            lax.ppermute(stage, "row_0", [(i, (i + s) % around) for i in range(around)])
            for s in range(1, around)
        ],
        axis=0,
    )
    nblk = coef_table.shape[0]
    both = jnp.concatenate([coef, direction], axis=1)
    neighbours = extended(both, (("day", 0),), 1)
    blks = blocks[0]
    span = count * local_blk
    rotated = ((there - blks // span) % around) * span + (
        (here - (blks // local_blk) % count) % count
    ) * local_blk
    selected = coef_table[rotated + blks % local_blk]
    feats = features[0]
    logits_dir = jnp.einsum("tari,taki->tkr", feats, selected, preferred_element_type=jnp.float32)
    logits = logits_dir[:, :arms]
    lin_dir = logits_dir[:, arms:]
    expo = jnp.exp(logits)
    probs = expo / jnp.sum(expo, axis=1, keepdims=True)
    onehot = (labels[0][:, None, :] == jnp.arange(arms, dtype=jnp.int32)[None, :, None]).astype(
        jnp.float32
    )
    resid = probs - onehot
    hrow = probs * lin_dir - probs * jnp.sum(probs * lin_dir, axis=1, keepdims=True)
    both_low = jnp.concatenate([resid, hrow], axis=1).astype(jnp.bfloat16)
    contrib = jnp.einsum("tari,tkr->taki", feats, both_low, preferred_element_type=jnp.float32)
    outer = lax.axis_size("row_0")
    inner = lax.axis_size("row_1")
    per = nblk // (outer * inner)
    flat = blks.reshape(-1)
    dest = ((flat // per) % inner) * (outer * per) + (flat // (inner * per)) * per + flat % per
    partial_terms = scatter_rows(dest, contrib, nblk)
    grad_part = partial_terms[:, :arms]
    hv_part = partial_terms[:, arms:].reshape(count, around, local_blk, arms, width)
    owned = lax.psum_scatter(grad_part, "row_1", scatter_dimension=0, tiled=True)
    chunks = owned.reshape(around, -1, arms, width)
    total = chunks[there]
    for s in range(1, around):
        total = total + lax.ppermute(
            chunks[(there + s) % around], "row_0", [(i, (i + s) % around) for i in range(around)]
        )
    across = hv_part[:, there]
    for s in range(1, around):
        across = across + lax.ppermute(
            hv_part[:, (there + s) % around], "row_0", [(i, (i + s) % around) for i in range(around)]
        )
    hv_total = across[here]
    for s in range(1, count):
        hv_total = hv_total + lax.ppermute(
            across[(here + s) % count], "row_1", [(i, (i + s) % count) for i in range(count)]
        )
    owned = jnp.concatenate([total, hv_total], axis=1)
    owned = owned.transpose(1, 0, 2).reshape(2 * arms, -1)
    day_index = lax.axis_index("day")
    ndays = lax.axis_size("day")
    links = (day_index > 0).astype(jnp.float32) + (day_index < ndays - 1).astype(jnp.float32)
    coupling = links * neighbours[1] - neighbours[0] - neighbours[2]
    result = owned + prior[None, :] * coupling
    return (result[None, :arms], result[None, arms:])


def solution(mesh):
    finer = Mesh(mesh.devices.reshape(mesh.shape["day"], 4, 8), ("day", "row_0", "row_1"))
    return jax.shard_map(
        on_device,
        mesh=finer,
        in_specs=(
            P("day", ROW, None, None, None),
            P("day", ROW, None),
            P("day", ROW, None),
            P("day", None, ROW),
            P("day", None, ROW),
            P(ROW),
        ),
        out_specs=(P("day", None, ROW), P("day", None, ROW)),
        check_vma=False,
    )
```

```python
import jax
import jax.numpy as jnp
from jax import lax
from jax.sharding import Mesh
from jax.sharding import PartitionSpec as P
from jax.experimental import pallas as pl
from jax.experimental.pallas import tpu as pltpu

ROW = ("row_0", "row_1")


def copy_for_each(value, axis):
    copies = jnp.broadcast_to(value, (lax.axis_size(axis), *value.shape))
    return lax.all_to_all(copies, axis, split_axis=0, concat_axis=0, tiled=True)


def extended(cells, sides, width):
    for axis, dim in sides:
        count = lax.axis_size(axis)
        ends = count - 1
        head = lax.slice_in_dim(cells, 0, width, axis=dim)
        tail = lax.slice_in_dim(cells, cells.shape[dim] - width, cells.shape[dim], axis=dim)
        cells = jnp.concatenate(
            [
                lax.ppermute(tail, axis, [(i, (i + 1) % count) for i in range(ends)]),
                cells,
                lax.ppermute(head, axis, [((i + 1) % count, i) for i in range(ends)]),
            ],
            axis=dim,
        )
    return cells


def scatter_axes(value, axes, dim):
    if not axes:
        return value
    nearer = lax.psum_scatter(value, axes[0], scatter_dimension=dim, tiled=True)
    return scatter_axes(nearer, axes[1:], dim)


def scatter_kernel(dest_ref, part_ref, out_ref):
    t = pl.program_id(0)
    slots = part_ref.shape[1]

    @pl.when(t == 0)
    def _():
        out_ref[...] = jnp.zeros_like(out_ref)

    for a in range(slots):
        q = dest_ref[t * slots + a]
        out_ref[q] = out_ref[q] + part_ref[0, a]


def scatter_rows(dest, contrib, nblk):
    tiles, slots, rows, width = contrib.shape
    return pl.pallas_call(
        scatter_kernel,
        grid_spec=pltpu.PrefetchScalarGridSpec(
            num_scalar_prefetch=1,
            grid=(tiles,),
            in_specs=[pl.BlockSpec((1, slots, rows, width), lambda t, d: (t, 0, 0, 0))],
            out_specs=pl.BlockSpec((nblk, rows, width), lambda t, d: (0, 0, 0)),
        ),
        out_shape=jax.ShapeDtypeStruct((nblk, rows, width), jnp.float32),
        compiler_params=pltpu.CompilerParams(
            dimension_semantics=("arbitrary",), vmem_limit_bytes=40 * 1024 * 1024
        ),
    )(dest, contrib)


def fused_kernel(dest_ref, feat_ref, sel_ref, lab_ref, out_ref):
    t = pl.program_id(0)
    slots = feat_ref.shape[1]
    arms = sel_ref.shape[2] // 2

    @pl.when(t == 0)
    def _():
        out_ref[...] = jnp.zeros_like(out_ref)

    acc = None
    for a in range(slots):
        part = lax.dot_general(
            sel_ref[0, a], feat_ref[0, a], (((1,), (1,)), ((), ())),
            preferred_element_type=jnp.float32,
        )
        acc = part if acc is None else acc + part
    logits = acc[:arms]
    lin_dir = acc[arms:]
    expo = jnp.exp(logits)
    probs = expo / jnp.sum(expo, axis=0, keepdims=True)
    arm_ids = lax.broadcasted_iota(jnp.int32, logits.shape, 0)
    onehot = (lab_ref[0] == arm_ids).astype(jnp.float32)
    resid = probs - onehot
    hrow = probs * lin_dir - probs * jnp.sum(probs * lin_dir, axis=0, keepdims=True)
    both_low = jnp.concatenate([resid, hrow], axis=0).astype(jnp.bfloat16)
    for a in range(slots):
        q = dest_ref[t * slots + a]
        out_ref[q] = out_ref[q] + jnp.dot(
            both_low, feat_ref[0, a], preferred_element_type=jnp.float32
        )


def fused_rows(dest, feats, selected, labels, nblk):
    tiles, slots, rows, width = feats.shape
    pair = selected.shape[2]
    return pl.pallas_call(
        fused_kernel,
        grid_spec=pltpu.PrefetchScalarGridSpec(
            num_scalar_prefetch=1,
            grid=(tiles,),
            in_specs=[
                pl.BlockSpec((1, slots, rows, width), lambda t, d: (t, 0, 0, 0)),
                pl.BlockSpec((1, slots, pair, width), lambda t, d: (t, 0, 0, 0)),
                pl.BlockSpec((1, 1, rows), lambda t, d: (t, 0, 0)),
            ],
            out_specs=pl.BlockSpec((nblk, pair, width), lambda t, d: (0, 0, 0)),
        ),
        out_shape=jax.ShapeDtypeStruct((nblk, pair, width), jnp.float32),
        compiler_params=pltpu.CompilerParams(
            dimension_semantics=("arbitrary",), vmem_limit_bytes=40 * 1024 * 1024
        ),
    )(dest, feats, selected, labels)


def on_device(features, blocks, labels, coef, direction, prior):
    arms = coef.shape[1]
    width = features.shape[-1]
    coef_pair = jnp.concatenate([coef[0], direction[0]], axis=0).astype(jnp.bfloat16)
    local_blk = coef_pair.shape[1] // width
    by_block = coef_pair.reshape(2 * arms, local_blk, width).transpose(1, 0, 2)
    here = lax.axis_index("row_1")
    count = lax.axis_size("row_1")
    pieces = [by_block] + [
        lax.ppermute(by_block, "row_1", [(i, (i + s) % count) for i in range(count)])
        for s in range(1, count)
    ]
    stage = jnp.concatenate(pieces, axis=0)
    there = lax.axis_index("row_0")
    around = lax.axis_size("row_0")
    coef_table = jnp.concatenate(
        [stage]
        + [
            lax.ppermute(stage, "row_0", [(i, (i + s) % around) for i in range(around)])
            for s in range(1, around)
        ],
        axis=0,
    )
    nblk = coef_table.shape[0]
    both = jnp.concatenate([coef, direction], axis=1)
    neighbours = extended(both, (("day", 0),), 1)
    blks = blocks[0]
    span = count * local_blk
    rotated = ((there - blks // span) % around) * span + (
        (here - (blks // local_blk) % count) % count
    ) * local_blk
    selected = coef_table[rotated + blks % local_blk]
    feats = features[0]
    outer = lax.axis_size("row_0")
    inner = lax.axis_size("row_1")
    per = nblk // (outer * inner)
    flat = blks.reshape(-1)
    dest = ((flat // per) % inner) * (outer * per) + (flat // (inner * per)) * per + flat % per
    partial_terms = fused_rows(dest, feats, selected, labels[0][:, None, :], nblk)
    grad_part = partial_terms[:, :arms]
    hv_part = partial_terms[:, arms:].reshape(count, around, local_blk, arms, width)
    owned = lax.psum_scatter(grad_part, "row_1", scatter_dimension=0, tiled=True)
    chunks = owned.reshape(around, -1, arms, width)
    total = chunks[there]
    for s in range(1, around):
        total = total + lax.ppermute(
            chunks[(there + s) % around], "row_0", [(i, (i + s) % around) for i in range(around)]
        )
    across = hv_part[:, there]
    for s in range(1, around):
        across = across + lax.ppermute(
            hv_part[:, (there + s) % around], "row_0", [(i, (i + s) % around) for i in range(around)]
        )
    hv_total = across[here]
    for s in range(1, count):
        hv_total = hv_total + lax.ppermute(
            across[(here + s) % count], "row_1", [(i, (i + s) % count) for i in range(count)]
        )
    owned = jnp.concatenate([total, hv_total], axis=1)
    owned = owned.transpose(1, 0, 2).reshape(2 * arms, -1)
    day_index = lax.axis_index("day")
    ndays = lax.axis_size("day")
    links = (day_index > 0).astype(jnp.float32) + (day_index < ndays - 1).astype(jnp.float32)
    coupling = links * neighbours[1] - neighbours[0] - neighbours[2]
    result = owned + prior[None, :] * coupling
    return (result[None, :arms], result[None, arms:])


def solution(mesh):
    finer = Mesh(mesh.devices.reshape(mesh.shape["day"], 4, 8), ("day", "row_0", "row_1"))
    return jax.shard_map(
        on_device,
        mesh=finer,
        in_specs=(
            P("day", ROW, None, None, None),
            P("day", ROW, None),
            P("day", ROW, None),
            P("day", None, ROW),
            P("day", None, ROW),
            P(ROW),
        ),
        out_specs=(P("day", None, ROW), P("day", None, ROW)),
        check_vma=False,
    )
```

```python
import jax
import jax.numpy as jnp
from jax import lax
from jax.sharding import Mesh
from jax.sharding import PartitionSpec as P
from jax.experimental import pallas as pl
from jax.experimental.pallas import tpu as pltpu

ROW = ("row_0", "row_1")


def copy_for_each(value, axis):
    copies = jnp.broadcast_to(value, (lax.axis_size(axis), *value.shape))
    return lax.all_to_all(copies, axis, split_axis=0, concat_axis=0, tiled=True)


def extended(cells, sides, width):
    for axis, dim in sides:
        count = lax.axis_size(axis)
        ends = count - 1
        head = lax.slice_in_dim(cells, 0, width, axis=dim)
        tail = lax.slice_in_dim(cells, cells.shape[dim] - width, cells.shape[dim], axis=dim)
        cells = jnp.concatenate(
            [
                lax.ppermute(tail, axis, [(i, (i + 1) % count) for i in range(ends)]),
                cells,
                lax.ppermute(head, axis, [((i + 1) % count, i) for i in range(ends)]),
            ],
            axis=dim,
        )
    return cells


def scatter_axes(value, axes, dim):
    if not axes:
        return value
    nearer = lax.psum_scatter(value, axes[0], scatter_dimension=dim, tiled=True)
    return scatter_axes(nearer, axes[1:], dim)


def scatter_kernel(dest_ref, part_ref, out_ref):
    t = pl.program_id(0)
    slots = part_ref.shape[1]

    @pl.when(t == 0)
    def _():
        out_ref[...] = jnp.zeros_like(out_ref)

    for a in range(slots):
        q = dest_ref[t * slots + a]
        out_ref[q] = out_ref[q] + part_ref[0, a]


def scatter_rows(dest, contrib, nblk):
    tiles, slots, rows, width = contrib.shape
    return pl.pallas_call(
        scatter_kernel,
        grid_spec=pltpu.PrefetchScalarGridSpec(
            num_scalar_prefetch=1,
            grid=(tiles,),
            in_specs=[pl.BlockSpec((1, slots, rows, width), lambda t, d: (t, 0, 0, 0))],
            out_specs=pl.BlockSpec((nblk, rows, width), lambda t, d: (0, 0, 0)),
        ),
        out_shape=jax.ShapeDtypeStruct((nblk, rows, width), jnp.float32),
        compiler_params=pltpu.CompilerParams(
            dimension_semantics=("arbitrary",), vmem_limit_bytes=40 * 1024 * 1024
        ),
    )(dest, contrib)


def on_device(features, blocks, labels, coef, direction, prior):
    arms = coef.shape[1]
    width = features.shape[-1]
    coef_pair = jnp.concatenate([coef[0], direction[0]], axis=0).astype(jnp.bfloat16)
    local_blk = coef_pair.shape[1] // width
    by_block = coef_pair.reshape(2 * arms, local_blk, width).transpose(1, 0, 2)
    here = lax.axis_index("row_1")
    count = lax.axis_size("row_1")
    pieces = [by_block] + [
        lax.ppermute(by_block, "row_1", [(i, (i + s) % count) for i in range(count)])
        for s in range(1, count)
    ]
    stage = jnp.concatenate(pieces, axis=0)
    there = lax.axis_index("row_0")
    around = lax.axis_size("row_0")
    coef_table = jnp.concatenate(
        [stage]
        + [
            lax.ppermute(stage, "row_0", [(i, (i + s) % around) for i in range(around)])
            for s in range(1, around)
        ],
        axis=0,
    )
    nblk = coef_table.shape[0]
    both = jnp.concatenate([coef, direction], axis=1)
    neighbours = extended(both, (("day", 0),), 1)
    blks = blocks[0]
    span = count * local_blk
    rotated = ((there - blks // span) % around) * span + (
        (here - (blks // local_blk) % count) % count
    ) * local_blk
    selected = coef_table[rotated + blks % local_blk]
    feats = features[0]
    logits_dir = jnp.einsum("tari,taki->tkr", feats, selected, preferred_element_type=jnp.float32)
    logits = logits_dir[:, :arms]
    lin_dir = logits_dir[:, arms:]
    expo = jnp.exp(logits)
    probs = expo / jnp.sum(expo, axis=1, keepdims=True)
    onehot = (labels[0][:, None, :] == jnp.arange(arms, dtype=jnp.int32)[None, :, None]).astype(
        jnp.float32
    )
    resid = probs - onehot
    hrow = probs * lin_dir - probs * jnp.sum(probs * lin_dir, axis=1, keepdims=True)
    both_low = jnp.concatenate([resid, hrow], axis=1).astype(jnp.bfloat16)
    contrib = jnp.einsum("tari,tkr->taki", feats, both_low, preferred_element_type=jnp.float32)
    outer = lax.axis_size("row_0")
    inner = lax.axis_size("row_1")
    per = nblk // (outer * inner)
    flat = blks.reshape(-1)
    dest = ((flat // per) % inner) * (outer * per) + (flat // (inner * per)) * per + flat % per
    partial_terms = scatter_rows(dest, contrib, nblk)
    cut = 3 * arms // 2
    grad_part = partial_terms[:, :cut]
    hv_part = partial_terms[:, cut:].reshape(count, around, local_blk, 2 * arms - cut, width)
    owned = lax.psum_scatter(grad_part, "row_1", scatter_dimension=0, tiled=True)
    chunks = owned.reshape(around, -1, cut, width)
    total = chunks[there]
    for s in range(1, around):
        total = total + lax.ppermute(
            chunks[(there + s) % around], "row_0", [(i, (i + s) % around) for i in range(around)]
        )
    across = hv_part[:, there]
    for s in range(1, around):
        across = across + lax.ppermute(
            hv_part[:, (there + s) % around], "row_0", [(i, (i + s) % around) for i in range(around)]
        )
    hv_total = across[here]
    for s in range(1, count):
        hv_total = hv_total + lax.ppermute(
            across[(here + s) % count], "row_1", [(i, (i + s) % count) for i in range(count)]
        )
    owned = jnp.concatenate([total, hv_total], axis=1)
    owned = owned.transpose(1, 0, 2).reshape(2 * arms, -1)
    day_index = lax.axis_index("day")
    ndays = lax.axis_size("day")
    links = (day_index > 0).astype(jnp.float32) + (day_index < ndays - 1).astype(jnp.float32)
    coupling = links * neighbours[1] - neighbours[0] - neighbours[2]
    result = owned + prior[None, :] * coupling
    return (result[None, :arms], result[None, arms:])


def solution(mesh):
    finer = Mesh(mesh.devices.reshape(mesh.shape["day"], 4, 8), ("day", "row_0", "row_1"))
    return jax.shard_map(
        on_device,
        mesh=finer,
        in_specs=(
            P("day", ROW, None, None, None),
            P("day", ROW, None),
            P("day", ROW, None),
            P("day", None, ROW),
            P("day", None, ROW),
            P(ROW),
        ),
        out_specs=(P("day", None, ROW), P("day", None, ROW)),
        check_vma=False,
    )
```
